128 devices in a mesh: amp: 16 (over x_hi, z, core), int: 8 (over x_lo, y).
Axes of the slice: x: 4 (x_hi: 2, x_lo: 2; x = x_hi * 2 + x_lo), y: 4, z: 4, core: 2. Of those that a mesh axis runs over, the one named last changes fastest.
Arguments:
- amplitudes: bfloat16 [1024, 384, 768], P('amp', None, 'int'), may hold values from -6 to 6
- integrals: bfloat16 [384, 768, 1536], P('amp', 'int'), may hold values from -0.015625 to 0.015625
- rest_residual: float32 [1024, 1536], P('amp', 'int'), may hold values from -6 to 6
- old_amplitudes: float32 [1024, 1536], P('amp', 'int'), may hold values from -3 to 3
- pair_energy: float32 [1024], P('amp'), may hold values from -4 to -1
- virt_energy: float32 [1536], P('int'), may hold values from 0.4 to 6
Outputs:
- new_amplitudes: float32 [1024, 1536], P('amp', 'int')
The draws below stay inside these ranges and needn't reach their ends.
All inputs are finite; a program needn't handle non-finite values.
Results may differ from the reference program's by a relative error of at most 0.0003.
Values may be sent and summed in bfloat16 or wider, within the bound.
No kernel may reach another device: no remote copies, remote signals or barrier semaphores. Data moves between devices by JAX's collectives and lax.ppermute only.
A program may use at most 128 MiB of HBM per device.

```python
import jax
import jax.numpy as jnp

D_VIRT = 768
PAIRS = 1024
CW = 384
AB = 1536


def with_spikes(entries, stream_key, source, target, blocks, factor):
    def block_of(position):
        return (jnp.arange(entries.shape[position]) // (entries.shape[position] // blocks)).reshape((-1,) + (1,) * (entries.ndim - 1 - position))

    first = jax.random.permutation(stream_key, blocks)[block_of(target)]
    far = (block_of(target) + blocks // 2) % blocks
    return jnp.where((block_of(source) == first) | (block_of(source) == far), factor * entries, entries)


def block_scale(stream_key, dims, pieces, least, largest):
    gain = 1.0
    for dim, parts in pieces:
        steps = jax.random.uniform(jax.random.fold_in(jax.random.fold_in(stream_key, 6), dim), (parts,), jnp.float32, least / len(pieces), largest / len(pieces))
        gain = gain * jnp.repeat(jnp.exp(steps), dims[dim] // parts).reshape((-1,) + (1,) * (len(dims) - 1 - dim))
    return gain


def noise(key, extent, width, bound, split=(), held_as=jnp.bfloat16):
    result = jax.random.normal(key, extent, jnp.float32) * width
    if len(split) > 0:
        result = block_scale(key, extent, split, -0.22, 0.18) * result
    return jnp.clip(result, min=-bound, max=bound).astype(held_as)


def bell_draw_with(stream_key, shape, spread, bound, pieces, heavy, kind=jnp.bfloat16):
    drawn = spread * jax.random.normal(stream_key, shape, jnp.float32)
    if pieces:
        drawn = drawn * block_scale(stream_key, shape, pieces, -0.22, 0.18)
    return jnp.clip(with_spikes(drawn, jax.random.fold_in(stream_key, 3), *heavy), -bound, bound).astype(kind)


def setup_inputs(seed: int = 0) -> dict:
    keys = jax.random.split(jax.random.key(seed), 7)
    return {
        "amplitudes": noise(keys[0], (PAIRS, CW, D_VIRT), 1.0, 6.0, ((0, 16), (2, 8))),
        "integrals": bell_draw_with(keys[1], (CW, D_VIRT, AB), (CW * D_VIRT) ** -0.5, 0.015625, ((0, 16), (1, 8)), (1, 2, 8, 2.0)),
        "rest_residual": noise(keys[2], (PAIRS, AB), 1.0, 6.0, ((0, 16), (1, 8)), jnp.float32),
        "old_amplitudes": noise(keys[3], (PAIRS, AB), 0.5, 3.0, ((0, 16), (1, 8)), jnp.float32),
        "pair_energy": jnp.clip(-4.0 + 3.0 * jax.random.uniform(keys[4], (PAIRS,), jnp.float32) ** block_scale(keys[4], (PAIRS,), ((0, 16),), -0.2, 0.2), -4.0, -1.0),
        "virt_energy": jnp.clip(0.4 + 5.6 * jax.random.uniform(keys[5], (AB,), jnp.float32) ** block_scale(keys[5], (AB,), ((0, 8),), -0.2, 0.2), 0.4, 6.0),
    }


def reference(amplitudes, integrals, rest_residual, old_amplitudes, pair_energy, virt_energy):
    ladder = jnp.dot(amplitudes.reshape(PAIRS, CW * D_VIRT), integrals.reshape(CW * D_VIRT, AB), preferred_element_type=jnp.float32)
    denominator = pair_energy[:, None] - virt_energy[None, :]
    return 0.4 * old_amplitudes + 0.6 * (ladder + rest_residual) / denominator
```

```python
import jax
import jax.numpy as jnp
from jax import lax
from jax.sharding import PartitionSpec as P


def scatter_sum(x, axis_name, axis):
    n = lax.axis_size(axis_name)
    me = lax.axis_index(axis_name)
    width = x.shape[axis] // n
    total = lax.dynamic_slice_in_dim(x, me * width, width, axis=axis)
    for s in range(1, n):
        block = lax.dynamic_slice_in_dim(x, ((me + s) % n) * width, width, axis=axis)
        total = total + lax.ppermute(block, axis_name, [(i, (i + s) % n) for i in range(n)])
    return total


def local(amplitudes, integrals, rest_residual, old_amplitudes, pair_energy, virt_energy):
    regrouped = lax.all_to_all(amplitudes, "amp", split_axis=1, concat_axis=0, tiled=True)
    partial = lax.dot_general(
        regrouped, integrals, (((1, 2), (0, 1)), ((), ())), preferred_element_type=jnp.float32
    )
    rows = lax.psum_scatter(partial, "amp", scatter_dimension=0, tiled=True)
    ladder = scatter_sum(rows, "int", 1)
    denominator = pair_energy[:, None] - virt_energy[None, :]
    return 0.4 * old_amplitudes + 0.6 * (ladder + rest_residual) / denominator


def solution(mesh):
    placed = (
        P("amp", None, "int"),
        P("amp", "int", None),
        P("amp", "int"),
        P("amp", "int"),
        P("amp"),
        P("int"),
    )
    return jax.shard_map(
        local, mesh=mesh, in_specs=placed, out_specs=P("amp", "int"), check_vma=False
    )
```

```python
import jax
import jax.numpy as jnp
from jax import lax
from jax.sharding import PartitionSpec as P


def scatter_sum(x, axis_name, axis):
    n = lax.axis_size(axis_name)
    me = lax.axis_index(axis_name)
    width = x.shape[axis] // n
    total = lax.dynamic_slice_in_dim(x, me * width, width, axis=axis)
    for s in range(1, n):
        block = lax.dynamic_slice_in_dim(x, ((me + s) % n) * width, width, axis=axis)
        total = total + lax.ppermute(block, axis_name, [(i, (i + s) % n) for i in range(n)])
    return total


def stage_sum(x, me_digit, size, stride, n):
    total = lax.dynamic_index_in_dim(x, me_digit, 0, keepdims=False)
    for s in range(1, size):
        block = lax.dynamic_index_in_dim(x, (me_digit + s) % size, 0, keepdims=False)
        perm = []
        for i in range(n):
            d = (i // stride) % size
            perm.append((i, i + (((d + s) % size) - d) * stride))
        total = total + lax.ppermute(block, "amp", perm)
    return total


def amp_reduce(partial, n_hi, n_z, n_core):
    n = n_hi * n_z * n_core
    me = lax.axis_index("amp")
    core = me % n_core
    z = (me // n_core) % n_z
    hi = me // (n_core * n_z)
    rows = partial.shape[0] // n
    x = partial.reshape(n_hi, n_z, n_core, rows, -1)
    x = stage_sum(jnp.moveaxis(x, 2, 0), core, n_core, 1, n)
    x = stage_sum(jnp.moveaxis(x, 1, 0), z, n_z, n_core, n)
    x = stage_sum(x, hi, n_hi, n_core * n_z, n)
    return x


def local(amplitudes, integrals, rest_residual, old_amplitudes, pair_energy, virt_energy):
    regrouped = lax.all_to_all(amplitudes, "amp", split_axis=1, concat_axis=0, tiled=True)
    partial = lax.dot_general(
        regrouped, integrals, (((1, 2), (0, 1)), ((), ())), preferred_element_type=jnp.float32
    )
    rows = amp_reduce(partial, 2, 4, 2)
    ladder = scatter_sum(rows, "int", 1)
    denominator = pair_energy[:, None] - virt_energy[None, :]
    return 0.4 * old_amplitudes + 0.6 * (ladder + rest_residual) / denominator


def solution(mesh):
    placed = (
        P("amp", None, "int"),
        P("amp", "int", None),
        P("amp", "int"),
        P("amp", "int"),
        P("amp"),
        P("int"),
    )
    return jax.shard_map(
        local, mesh=mesh, in_specs=placed, out_specs=P("amp", "int"), check_vma=False
    )
```

```python
import jax
import jax.numpy as jnp
from jax import lax
from jax.sharding import PartitionSpec as P

CHUNKS = 2


def scatter_sum(x, axis_name, axis):
    n = lax.axis_size(axis_name)
    me = lax.axis_index(axis_name)
    width = x.shape[axis] // n
    total = lax.dynamic_slice_in_dim(x, me * width, width, axis=axis)
    for s in range(1, n):
        block = lax.dynamic_slice_in_dim(x, ((me + s) % n) * width, width, axis=axis)
        total = total + lax.ppermute(block, axis_name, [(i, (i + s) % n) for i in range(n)])
    return total


def stage_sum(x, me_digit, size, stride, n):
    total = lax.dynamic_index_in_dim(x, me_digit, 0, keepdims=False)
    for s in range(1, size):
        block = lax.dynamic_index_in_dim(x, (me_digit + s) % size, 0, keepdims=False)
        perm = []
        for i in range(n):
            d = (i // stride) % size
            perm.append((i, i + (((d + s) % size) - d) * stride))
        total = total + lax.ppermute(block, "amp", perm)
    return total


def amp_reduce(partial, n_hi, n_z, n_core):
    n = n_hi * n_z * n_core
    me = lax.axis_index("amp")
    core = me % n_core
    z = (me // n_core) % n_z
    hi = me // (n_core * n_z)
    rows = partial.shape[0] // n
    x = partial.reshape(n_hi, n_z, n_core, rows, -1)
    x = stage_sum(jnp.moveaxis(x, 2, 0), core, n_core, 1, n)
    x = stage_sum(jnp.moveaxis(x, 1, 0), z, n_z, n_core, n)
    x = stage_sum(x, hi, n_hi, n_core * n_z, n)
    return x


def local(amplitudes, integrals, rest_residual, old_amplitudes, pair_energy, virt_energy):
    pairs = amplitudes.shape[0]
    step = pairs // CHUNKS
    pieces = []
    for k in range(CHUNKS):
        part = amplitudes[k * step:(k + 1) * step]
        regrouped = lax.all_to_all(part, "amp", split_axis=1, concat_axis=0, tiled=True)
        partial = lax.dot_general(
            regrouped, integrals, (((1, 2), (0, 1)), ((), ())), preferred_element_type=jnp.float32
        )
        pieces.append(amp_reduce(partial, 2, 4, 2))
    rows = jnp.concatenate(pieces, axis=0)
    ladder = scatter_sum(rows, "int", 1)
    denominator = pair_energy[:, None] - virt_energy[None, :]
    return 0.4 * old_amplitudes + 0.6 * (ladder + rest_residual) / denominator


def solution(mesh):
    placed = (
        P("amp", None, "int"),
        P("amp", "int", None),
        P("amp", "int"),
        P("amp", "int"),
        P("amp"),
        P("int"),
    )
    return jax.shard_map(
        local, mesh=mesh, in_specs=placed, out_specs=P("amp", "int"), check_vma=False
    )
```

```python
import jax
import jax.numpy as jnp
from jax import lax
from jax.sharding import PartitionSpec as P

CHUNKS = 3


def scatter_sum(x, axis_name, axis):
    n = lax.axis_size(axis_name)
    me = lax.axis_index(axis_name)
    width = x.shape[axis] // n
    total = lax.dynamic_slice_in_dim(x, me * width, width, axis=axis)
    for s in range(1, n):
        block = lax.dynamic_slice_in_dim(x, ((me + s) % n) * width, width, axis=axis)
        total = total + lax.ppermute(block, axis_name, [(i, (i + s) % n) for i in range(n)])
    return total


def stage_sum(x, me_digit, size, stride, n):
    total = lax.dynamic_index_in_dim(x, me_digit, 0, keepdims=False)
    for s in range(1, size):
        block = lax.dynamic_index_in_dim(x, (me_digit + s) % size, 0, keepdims=False)
        perm = []
        for i in range(n):
            d = (i // stride) % size
            perm.append((i, i + (((d + s) % size) - d) * stride))
        total = total + lax.ppermute(block, "amp", perm)
    return total


def amp_reduce(partial, n_hi, n_z, n_core):
    n = n_hi * n_z * n_core
    me = lax.axis_index("amp")
    core = me % n_core
    z = (me // n_core) % n_z
    hi = me // (n_core * n_z)
    rows = partial.shape[0] // n
    x = partial.reshape(n_hi, n_z, n_core, rows, -1)
    x = stage_sum(jnp.moveaxis(x, 2, 0), core, n_core, 1, n)
    x = stage_sum(jnp.moveaxis(x, 1, 0), z, n_z, n_core, n)
    x = stage_sum(x, hi, n_hi, n_core * n_z, n)
    return x


def local(amplitudes, integrals, rest_residual, old_amplitudes, pair_energy, virt_energy):
    pairs = amplitudes.shape[0]
    sizes = (24, 24, 16)
    pieces = []
    for k in range(CHUNKS):
        part = amplitudes[sum(sizes[:k]):sum(sizes[:k + 1])]
        regrouped = lax.all_to_all(part, "amp", split_axis=1, concat_axis=0, tiled=True)
        partial = lax.dot_general(
            regrouped, integrals, (((1, 2), (0, 1)), ((), ())), preferred_element_type=jnp.float32
        )
        pieces.append(amp_reduce(partial, 2, 4, 2))
    rows = jnp.concatenate(pieces, axis=0)
    ladder = scatter_sum(rows, "int", 1)
    denominator = pair_energy[:, None] - virt_energy[None, :]
    return 0.4 * old_amplitudes + 0.6 * (ladder + rest_residual) / denominator


def solution(mesh):
    placed = (
        P("amp", None, "int"),
        P("amp", "int", None),
        P("amp", "int"),
        P("amp", "int"),
        P("amp"),
        P("int"),
    )
    return jax.shard_map(
        local, mesh=mesh, in_specs=placed, out_specs=P("amp", "int"), check_vma=False
    )
```

```python
import jax
import jax.numpy as jnp
from jax import lax
from jax.sharding import PartitionSpec as P

SIZES = (24, 24, 16)


def stage_sum(x, me_digit, size, stride, n):
    total = lax.dynamic_index_in_dim(x, me_digit, 0, keepdims=False)
    for s in range(1, size):
        block = lax.dynamic_index_in_dim(x, (me_digit + s) % size, 0, keepdims=False)
        perm = []
        for i in range(n):
            d = (i // stride) % size
            perm.append((i, i + (((d + s) % size) - d) * stride))
        total = total + lax.ppermute(block, "amp", perm)
    return total


def local(amplitudes, integrals, rest_residual, old_amplitudes, pair_energy, virt_energy):
    n_hi, n_z, n_core = 2, 4, 2
    n = n_hi * n_z * n_core
    n_chips = n // n_core
    me = lax.axis_index("amp")
    core = me % n_core
    z = (me // n_core) % n_z
    hi = me // (n_core * n_z)
    pairs, cw, dl = amplitudes.shape
    width = cw // n
    sibling = lax.ppermute(integrals, "amp", [(i, i ^ 1) for i in range(n)])
    groups = [[c + n_core * m for m in range(n_chips)] for c in range(n_core)]
    dims = (((1, 2), (0, 1)), ((), ()))
    pieces = []
    start = 0
    for size in SIZES:
        part = amplitudes[start:start + size]
        start += size
        got = lax.all_to_all(
            part, "amp", split_axis=1, concat_axis=0, tiled=True, axis_index_groups=groups
        )
        own = lax.dynamic_slice_in_dim(got, core * width, width, axis=1)
        other = lax.dynamic_slice_in_dim(got, (1 - core) * width, width, axis=1)
        partial = lax.dot_general(own, integrals, dims, preferred_element_type=jnp.float32)
        partial = partial + lax.dot_general(other, sibling, dims, preferred_element_type=jnp.float32)
        x = partial.reshape(n_hi, n_z, size, -1)
        x = stage_sum(jnp.moveaxis(x, 1, 0), z, n_z, n_core, n)
        pieces.append(stage_sum(x, hi, n_hi, n_core * n_z, n))
    rows = jnp.concatenate(pieces, axis=0)
    n_int = lax.axis_size("int")
    blocks = rows.reshape(rows.shape[0], n_int, -1)
    ladder = lax.all_to_all(blocks, "int", split_axis=1, concat_axis=1, tiled=True).sum(axis=1)
    denominator = pair_energy[:, None] - virt_energy[None, :]
    return 0.4 * old_amplitudes + 0.6 * (ladder + rest_residual) / denominator


def solution(mesh):
    placed = (
        P("amp", None, "int"),
        P("amp", "int", None),
        P("amp", "int"),
        P("amp", "int"),
        P("amp"),
        P("int"),
    )
    return jax.shard_map(
        local, mesh=mesh, in_specs=placed, out_specs=P("amp", "int"), check_vma=False
    )
```

```python
import jax
import jax.numpy as jnp
from jax import lax
from jax.sharding import PartitionSpec as P

SIZES = (40, 24)


def stage_sum(x, me_digit, size, stride, n):
    total = lax.dynamic_index_in_dim(x, me_digit, 0, keepdims=False)
    for s in range(1, size):
        block = lax.dynamic_index_in_dim(x, (me_digit + s) % size, 0, keepdims=False)
        perm = []
        for i in range(n):
            d = (i // stride) % size
            perm.append((i, i + (((d + s) % size) - d) * stride))
        total = total + lax.ppermute(block, "amp", perm)
    return total


def local(amplitudes, integrals, rest_residual, old_amplitudes, pair_energy, virt_energy):
    n_hi, n_z, n_core = 2, 4, 2
    n = n_hi * n_z * n_core
    n_chips = n // n_core
    me = lax.axis_index("amp")
    core = me % n_core
    z = (me // n_core) % n_z
    hi = me // (n_core * n_z)
    pairs, cw, dl = amplitudes.shape
    width = cw // n
    sibling = lax.ppermute(integrals, "amp", [(i, i ^ 1) for i in range(n)])
    groups = [[c + n_core * m for m in range(n_chips)] for c in range(n_core)]
    dims = (((1, 2), (0, 1)), ((), ()))
    pieces = []
    start = 0
    for size in SIZES:
        part = amplitudes[start:start + size]
        start += size
        got = lax.all_to_all(
            part, "amp", split_axis=1, concat_axis=0, tiled=True, axis_index_groups=groups
        )
        own = lax.dynamic_slice_in_dim(got, core * width, width, axis=1)
        other = lax.dynamic_slice_in_dim(got, (1 - core) * width, width, axis=1)
        partial = lax.dot_general(own, integrals, dims, preferred_element_type=jnp.float32)
        partial = partial + lax.dot_general(other, sibling, dims, preferred_element_type=jnp.float32)
        x = partial.reshape(n_hi, n_z, size, -1)
        x = stage_sum(jnp.moveaxis(x, 1, 0), z, n_z, n_core, n)
        pieces.append(stage_sum(x, hi, n_hi, n_core * n_z, n))
    rows = jnp.concatenate(pieces, axis=0)
    n_int = lax.axis_size("int")
    blocks = rows.reshape(rows.shape[0], n_int, -1)
    ladder = lax.all_to_all(blocks, "int", split_axis=1, concat_axis=1, tiled=True).sum(axis=1)
    denominator = pair_energy[:, None] - virt_energy[None, :]
    return 0.4 * old_amplitudes + 0.6 * (ladder + rest_residual) / denominator


def solution(mesh):
    placed = (
        P("amp", None, "int"),
        P("amp", "int", None),
        P("amp", "int"),
        P("amp", "int"),
        P("amp"),
        P("int"),
    )
    return jax.shard_map(
        local, mesh=mesh, in_specs=placed, out_specs=P("amp", "int"), check_vma=False
    )
```

```python
import jax
import jax.numpy as jnp
from jax import lax
from jax.sharding import PartitionSpec as P

SIZES = (40, 24)


def stage_sum(x, me_digit, size, stride, n):
    total = lax.dynamic_index_in_dim(x, me_digit, 0, keepdims=False)
    for s in range(1, size):
        block = lax.dynamic_index_in_dim(x, (me_digit + s) % size, 0, keepdims=False)
        perm = []
        for i in range(n):
            d = (i // stride) % size
            perm.append((i, i + (((d + s) % size) - d) * stride))
        total = total + lax.ppermute(block, "amp", perm)
    return total


def local(amplitudes, integrals, rest_residual, old_amplitudes, pair_energy, virt_energy):
    n_hi, n_z, n_core = 2, 4, 2
    n = n_hi * n_z * n_core
    n_chips = n // n_core
    me = lax.axis_index("amp")
    core = me % n_core
    z = (me // n_core) % n_z
    hi = me // (n_core * n_z)
    pairs, cw, dl = amplitudes.shape
    width = cw // n
    sibling = lax.ppermute(integrals, "amp", [(i, i ^ 1) for i in range(n)])
    groups = [[c + n_core * m for m in range(n_chips)] for c in range(n_core)]
    dims = (((1, 2), (0, 1)), ((), ()))
    pieces = []
    start = 0
    def reduce(partial):
        x = partial.reshape(n_hi, n_z, -1, partial.shape[-1])
        x = stage_sum(jnp.moveaxis(x, 1, 0), z, n_z, n_core, n)
        return stage_sum(x, hi, n_hi, n_core * n_z, n)

    prev = None
    for size in SIZES:
        part = amplitudes[start:start + size]
        start += size
        if prev is not None:
            prev, part = lax.optimization_barrier((prev, part))
            pieces.append(reduce(prev))
        got = lax.all_to_all(
            part, "amp", split_axis=1, concat_axis=0, tiled=True, axis_index_groups=groups
        )
        own = lax.dynamic_slice_in_dim(got, core * width, width, axis=1)
        other = lax.dynamic_slice_in_dim(got, (1 - core) * width, width, axis=1)
        partial = lax.dot_general(own, integrals, dims, preferred_element_type=jnp.float32)
        prev = partial + lax.dot_general(other, sibling, dims, preferred_element_type=jnp.float32)
    pieces.append(reduce(prev))
    rows = jnp.concatenate(pieces, axis=0)
    n_int = lax.axis_size("int")
    blocks = rows.reshape(rows.shape[0], n_int, -1)
    ladder = lax.all_to_all(blocks, "int", split_axis=1, concat_axis=1, tiled=True).sum(axis=1)
    denominator = pair_energy[:, None] - virt_energy[None, :]
    return 0.4 * old_amplitudes + 0.6 * (ladder + rest_residual) / denominator


def solution(mesh):
    placed = (
        P("amp", None, "int"),
        P("amp", "int", None),
        P("amp", "int"),
        P("amp", "int"),
        P("amp"),
        P("int"),
    )
    return jax.shard_map(
        local, mesh=mesh, in_specs=placed, out_specs=P("amp", "int"), check_vma=False
    )
```
